1024 devices in a mesh: dp: 64 (over y, x), bytes: 16 (over z, core).
Axes of the slice: x: 8, y: 8, z: 8, core: 2. Of those that a mesh axis runs over, the one named last changes fastest.
Arguments:
- byte_queries: bfloat16 [64, 2048, 1024], P('dp', 'bytes'), may hold values from -48 to 48
- byte_keys: bfloat16 [64, 2048, 1024], P('dp', 'bytes'), may hold values from -6 to 6
- byte_values: bfloat16 [64, 2048, 1024], P('dp', 'bytes'), may hold values from -6 to 6
- patch_starts: int32 [64, 16, 12], P('dp', 'bytes'), may hold values from 0 to 128, as said below
- patch_proj: bfloat16 [1024, 4096], P('dp', 'bytes'), may hold values from -0.1875 to 0.1875
- latent_proj: bfloat16 [4096, 4096], P('bytes', 'dp'), may hold values from -0.09375 to 0.09375
- latent_cotangent: bfloat16 [64, 192, 4096], P('dp', 'bytes'), may hold values from -6 to 6
Outputs:
- latent_out: bfloat16 [64, 192, 4096], P('dp', 'bytes')
- pooled_grad: bfloat16 [64, 192, 1024], P('dp', 'bytes')
The draws below stay inside these ranges and needn't reach their ends.
Inputs may be any that keep to these rules, and one draw needn't show every extreme that they name: `patch_starts`: per shard the first entry is 0, entries increase strictly while below 128 and the rest equal 128; a shard has 6 to 12 patches, and in every stream some shard has exactly 12.
All inputs are finite; a program needn't handle non-finite values.
Results may differ from the reference program's by a relative error of at most 0.025.
Values may be sent and summed in bfloat16 or wider, within the bound.
No kernel may reach another device: no remote copies, remote signals or barrier semaphores. Data moves between devices by JAX's collectives and lax.ppermute only.
A program may use at most 32 MiB of HBM per device.

```python
import jax
import jax.numpy as jnp
from jax import lax

DL = 1024
HEAD_L = 64
D = 4096
B_DEV = 128
HEADS_L = 16
PCAP = 12
WIN = 256
STREAMS = 64
SEQ = 2048
PATCHES = 192
N_BYTES = 16


def key_jitter(key):
    return jnp.clip(jax.random.normal(jax.random.fold_in(key, 11), (STREAMS, SEQ, DL), jnp.float32), -6.0, 6.0)


def draw_byte_keys(key, part):
    base = key_jitter(key)
    return base.astype(jnp.bfloat16)


def draw_byte_queries(key, part):
    return jnp.clip(jax.random.normal(jax.random.fold_in(key, 13), (STREAMS, SEQ, DL), jnp.float32), -6.0, 6.0).astype(jnp.bfloat16)


def draw_patch_starts(key, part):
    base = jax.random.fold_in(key, 3)
    first_key, count_key, order_key = jax.random.split(base, 3)
    full = jax.random.randint(first_key, (STREAMS, 1), 0, N_BYTES)
    counts = jax.random.randint(count_key, (STREAMS, N_BYTES), PCAP // 2, PCAP + 1)
    counts = jnp.where(jnp.arange(N_BYTES, dtype=jnp.int32)[None, :] == full, PCAP, counts)
    scores = jax.random.randint(order_key, (STREAMS, N_BYTES, B_DEV - 1), 0, 2 ** 20)
    scores = scores * B_DEV + jnp.arange(B_DEV - 1, dtype=jnp.int32)[None, None, :]
    order = jnp.argsort(scores, axis=-1, stable=True).astype(jnp.int32)
    picks = order[:, :, :PCAP - 1] + 1
    slots = jnp.arange(PCAP - 1, dtype=jnp.int32)[None, None, :]
    picks = jnp.where(slots < counts[:, :, None] - 1, picks, B_DEV)
    picks = jnp.sort(picks, axis=-1)
    zeros = jnp.zeros((STREAMS, N_BYTES, 1), jnp.int32)
    return jnp.concatenate([zeros, picks], axis=-1).astype(jnp.int32)


def block_levels(stream_key, dims, cuts, low, largest):
    factor_of, own = 1.0, jax.random.fold_in(stream_key, 6)
    for position, shards_of in cuts:
        draws = jnp.exp(jax.random.uniform(jax.random.fold_in(own, position), (shards_of,), jnp.float32, low / len(cuts), largest / len(cuts)))
        factor_of = factor_of * jnp.repeat(draws, dims[position] // shards_of).reshape([-1 if axis == position else 1 for axis in range(len(dims))])
    return factor_of


def noise(own_key, dims, spread, most, pieces=(), kind=jnp.bfloat16):
    entries = spread * jax.random.normal(own_key, dims, jnp.float32)
    if pieces:
        entries = entries * block_levels(own_key, dims, pieces, -0.22, 0.18)
    return jnp.clip(entries, -most, most).astype(kind)


def setup_inputs(seed: int = 0) -> dict:
    key_list = jax.random.split(jax.random.key(seed), 8)
    byte_queries = draw_byte_queries(jax.random.fold_in(key_list[7], 71), 0)
    byte_keys = draw_byte_keys(jax.random.fold_in(key_list[7], 71), 0)
    byte_values = noise(key_list[2], (STREAMS, SEQ, DL), 1.0, 6.0, ((0, 64), (1, 16)))
    patch_starts = draw_patch_starts(jax.random.fold_in(key_list[7], 71), 0)
    patch_proj = noise(key_list[4], (DL, D), DL ** -0.5, 0.1875, ((0, 64), (1, 16)))
    latent_proj = noise(key_list[5], (D, D), D ** -0.5, 0.09375, ((0, 16), (1, 64)))
    latent_cotangent = noise(key_list[6], (STREAMS, PATCHES, D), 1.0, 6.0, ((0, 64), (1, 16)))
    return {"byte_queries": byte_queries, "byte_keys": byte_keys, "byte_values": byte_values, "patch_starts": patch_starts, "patch_proj": patch_proj, "latent_proj": latent_proj, "latent_cotangent": latent_cotangent}


def encode(query, keys, values):
    shape = (N_BYTES, B_DEV, HEADS_L, HEAD_L)
    qb = query.reshape(shape).astype(jnp.float32)
    kb = keys.reshape(shape).astype(jnp.float32)
    vb = values.reshape(shape).astype(jnp.float32)
    k_one = jnp.concatenate([jnp.zeros_like(kb[:1]), kb[:-1]], axis=0)
    v_one = jnp.concatenate([jnp.zeros_like(vb[:1]), vb[:-1]], axis=0)
    k_two = jnp.concatenate([jnp.zeros_like(kb[:2]), kb[:-2]], axis=0)
    v_two = jnp.concatenate([jnp.zeros_like(vb[:2]), vb[:-2]], axis=0)
    k_all = jnp.concatenate([k_two, k_one, kb], axis=1)
    v_all = jnp.concatenate([v_two, v_one, vb], axis=1)
    scores = jnp.einsum("nihd,njhd->nhij", qb, k_all) * (HEAD_L ** -0.5)
    qpos = jnp.arange(B_DEV, dtype=jnp.int32)[:, None] + 2 * B_DEV
    kpos = jnp.arange(3 * B_DEV, dtype=jnp.int32)[None, :]
    inside = (kpos <= qpos) & (kpos > qpos - WIN)
    shard = jnp.arange(N_BYTES, dtype=jnp.int32)[:, None, None, None]
    kp = kpos[None, None]
    reach = (kp >= 2 * B_DEV) | ((kp >= B_DEV) & (shard >= 1)) | (shard >= 2)
    allowed = inside[None, None] & reach
    scores = jnp.where(allowed, scores, -1e30)
    top = jnp.max(scores, axis=-1, keepdims=True)
    expo = jnp.exp(scores - top)
    weights = (expo / jnp.sum(expo, axis=-1, keepdims=True)).astype(jnp.bfloat16)
    encoded = jnp.einsum("nhij,njhd->nihd", weights.astype(jnp.float32), v_all)
    return encoded.astype(jnp.bfloat16).reshape(N_BYTES, B_DEV, DL)


def pool(encoded, starts):
    nexts = jnp.concatenate([starts[:, 1:], jnp.full((N_BYTES, 1), B_DEV, jnp.int32)], axis=1)
    place = jnp.arange(B_DEV, dtype=jnp.int32)[None, None, :]
    member = (place >= starts[:, :, None]) & (place < nexts[:, :, None])
    length = jnp.sum(member.astype(jnp.float32), axis=-1)
    summed = jnp.einsum("npb,nbd->npd", member.astype(jnp.float32), encoded.astype(jnp.float32))
    pooled = summed / jnp.maximum(length, 1.0)[..., None]
    return pooled.astype(jnp.bfloat16).reshape(PATCHES, DL)


def one_stream(items, patch_proj, latent_proj):
    query, keys, values, starts, cotangent = items
    pooled = pool(encode(query, keys, values), starts)
    valid = (starts < B_DEV).reshape(PATCHES)
    block = D // N_BYTES
    hidden_in = jnp.dot(pooled, patch_proj, preferred_element_type=jnp.float32)
    activation = jax.nn.silu(hidden_in).astype(jnp.bfloat16)
    activation_tiles = activation.reshape(PATCHES, N_BYTES, block).transpose(1, 0, 2).astype(jnp.float32)
    weight_tiles = latent_proj.reshape(N_BYTES, block, D).astype(jnp.float32)
    part_pieces = jnp.einsum("foy,fyw->fow", activation_tiles, weight_tiles).astype(jnp.bfloat16)
    part_pieces = lax.optimization_barrier(part_pieces).astype(jnp.float32)
    latent_out = jnp.sum(part_pieces, axis=0).astype(jnp.bfloat16)
    back = jnp.dot(cotangent, latent_proj.T, preferred_element_type=jnp.float32)
    sigma = jax.nn.sigmoid(hidden_in)
    act_grad = (back * sigma * (1.0 + hidden_in * (1.0 - sigma))).astype(jnp.bfloat16)
    grad_blocks = act_grad.reshape(PATCHES, N_BYTES, block).transpose(1, 0, 2).astype(jnp.float32)
    proj_blocks = patch_proj.reshape(DL, N_BYTES, block).transpose(1, 0, 2).astype(jnp.float32)
    gparts = jnp.einsum("bpk,bek->bpe", grad_blocks, proj_blocks).astype(jnp.bfloat16)
    gparts = lax.optimization_barrier(gparts).astype(jnp.float32)
    pooled_grad = jnp.where(valid[:, None], jnp.sum(gparts, axis=0), 0.0).astype(jnp.bfloat16)
    return latent_out, pooled_grad


def reference(byte_queries, byte_keys, byte_values, patch_starts, patch_proj, latent_proj, latent_cotangent):
    def step(items):
        return one_stream(items, patch_proj, latent_proj)

    latent_out, pooled_grad = lax.map(step, (byte_queries, byte_keys, byte_values, patch_starts, latent_cotangent))
    return latent_out, pooled_grad
```

```python
import math

import jax
import jax.numpy as jnp
import numpy as np
from jax import lax
from jax.sharding import Mesh
from jax.sharding import PartitionSpec as P

HEAD_L = 64
BYTE_AXES = ("z", "c")
DP_AXES = ("y", "x")


def shifted(shard, axis, by):
    devices = lax.axis_size(axis)
    pairs = [(i, i + by) for i in range(devices) if 0 <= i + by < devices]
    return lax.ppermute(shard, axis, pairs)


def per_device(
    byte_queries, byte_keys, byte_values, patch_starts, patch_proj, latent_proj, latent_cotangent
):
    rows = byte_queries.shape[1]
    width = byte_queries.shape[2]
    heads = width // HEAD_L
    group_size = math.gcd(heads, 4)
    groups = heads // group_size

    proj_rows, block = patch_proj.shape
    lat_rows, lat_cols = latent_proj.shape
    wbuf = jnp.concatenate([patch_proj.reshape(-1), latent_proj.reshape(-1)])
    wbuf = lax.all_gather(wbuf, "x", axis=0)
    wbuf = lax.all_gather(wbuf, "y", axis=0)
    ndp = wbuf.shape[0] * wbuf.shape[1]
    wbuf = wbuf.reshape(ndp, -1)
    proj_cols = wbuf[:, : proj_rows * block].reshape(ndp * proj_rows, block)
    latent_w = wbuf[:, proj_rows * block :].reshape(ndp, lat_rows, lat_cols)

    cot = lax.all_gather(latent_cotangent[0], "z", axis=0, tiled=True)
    cot_all = lax.all_gather(cot, "c", axis=0, tiled=True)

    received = {}
    for reach in (2, 1):
        received[reach] = shifted((byte_keys, byte_values), BYTE_AXES, reach)
    keys_all = jnp.concatenate([received[2][0][0], received[1][0][0], byte_keys[0]], axis=0)
    values_all = jnp.concatenate([received[2][1][0], received[1][1][0], byte_values[0]], axis=0)
    query_groups = byte_queries[0].reshape(rows, groups, group_size, HEAD_L).transpose(1, 0, 2, 3)
    key_groups = keys_all.reshape(3 * rows, groups, group_size, HEAD_L).transpose(1, 0, 2, 3)
    value_group_list = values_all.reshape(3 * rows, groups, group_size, HEAD_L).transpose(
        1, 0, 2, 3
    )
    qpos = jnp.arange(rows, dtype=jnp.int32)[:, None] + 2 * rows
    kpos = jnp.arange(3 * rows, dtype=jnp.int32)[None, :]
    position = lax.axis_index(BYTE_AXES)
    reachable = (kpos >= 2 * rows) | (kpos >= rows) & (position >= 1) | (position >= 2)
    allowed = (kpos <= qpos) & (kpos > qpos - 2 * rows) & reachable

    def attend(items):
        query, keys, values = items
        scores = jnp.einsum(
            "ihd,jhd->hij", query, keys, preferred_element_type=jnp.float32
        ) * HEAD_L ** (-0.5)
        scores = jnp.where(allowed[None], scores, -1e30)
        top = jnp.max(scores, axis=-1, keepdims=True)
        expo = jnp.exp(scores - top)
        weights = (expo / jnp.sum(expo, axis=-1, keepdims=True)).astype(jnp.bfloat16)
        mixed = jnp.einsum("hij,jhd->ihd", weights, values, preferred_element_type=jnp.float32)
        return mixed.astype(jnp.bfloat16)

    encoded = lax.map(attend, (query_groups, key_groups, value_group_list))
    encoded = encoded.transpose(1, 0, 2, 3).reshape(rows, width)
    starts = patch_starts[0, 0]
    nexts = jnp.concatenate([starts[1:], jnp.full((1,), rows, jnp.int32)])
    place = jnp.arange(rows, dtype=jnp.int32)[None, :]
    member = (place >= starts[:, None]) & (place < nexts[:, None])
    length = jnp.sum(member.astype(jnp.float32), axis=-1)
    summed = jnp.dot(member.astype(jnp.bfloat16), encoded, preferred_element_type=jnp.float32)
    pooled = (summed / jnp.maximum(length, 1.0)[:, None]).astype(jnp.bfloat16)
    valid = starts < rows

    patches = lax.all_gather(pooled, "z", axis=0, tiled=True)
    patches = lax.all_gather(patches, "c", axis=0, tiled=True)
    hidden_in = jnp.dot(patches, proj_cols, preferred_element_type=jnp.float32)
    activation = jax.nn.silu(hidden_in).astype(jnp.bfloat16)
    latent_part = jnp.einsum(
        "pk,dkj->pdj", activation, latent_w, preferred_element_type=jnp.float32
    ).astype(jnp.bfloat16)
    latent_part = latent_part.reshape(latent_part.shape[0], -1)
    latent = lax.psum_scatter(latent_part, "c", scatter_dimension=0, tiled=True)
    latent = lax.psum_scatter(latent, "z", scatter_dimension=0, tiled=True)

    cot_all = cot_all.reshape(cot_all.shape[0], ndp, lat_cols)
    back = jnp.einsum("pdj,dkj->pk", cot_all, latent_w, preferred_element_type=jnp.float32)
    sigma = jax.nn.sigmoid(hidden_in)
    act_grad = (back * sigma * (1.0 + hidden_in * (1.0 - sigma))).astype(jnp.bfloat16)
    gpart = lax.dot_general(
        act_grad, proj_cols, (((1,), (1,)), ((), ())), preferred_element_type=jnp.float32
    ).astype(jnp.bfloat16)
    grads = lax.psum_scatter(gpart, "c", scatter_dimension=0, tiled=True)
    grads = lax.psum_scatter(grads, "z", scatter_dimension=0, tiled=True).astype(jnp.float32)
    grads = jnp.where(valid[:, None], grads, 0.0)
    return (latent[None], grads.astype(jnp.bfloat16)[None])


def solution(mesh):
    n_dp = mesh.shape["dp"]
    n_bytes = mesh.shape["bytes"]
    side = int(round(math.sqrt(n_dp)))
    view = Mesh(
        np.asarray(mesh.devices).reshape(n_dp // side, side, n_bytes // 2, 2),
        DP_AXES + BYTE_AXES,
    )
    act = P(DP_AXES, BYTE_AXES, None)
    return jax.shard_map(
        per_device,
        mesh=view,
        in_specs=(act, act, act, act, P(DP_AXES, BYTE_AXES), P(BYTE_AXES, DP_AXES), act),
        out_specs=(act, act),
        check_vma=False,
    )
```

```python
import math

import jax
import jax.numpy as jnp
from jax import lax
import numpy as np
from jax.sharding import Mesh
from jax.sharding import PartitionSpec as P

HEAD_L = 64
BYTE_AXES = ("z", "c")
DP_AXES = ("y", "x")


def shifted(shard, axis, by):
    devices = lax.axis_size(axis)
    pairs = [(i, i + by) for i in range(devices) if 0 <= i + by < devices]
    return lax.ppermute(shard, axis, pairs)


def per_device(
    byte_queries, byte_keys, byte_values, patch_starts, patch_proj, latent_proj, latent_cotangent
):
    rows = byte_queries.shape[1]
    width = byte_queries.shape[2]
    heads = width // HEAD_L
    group_size = math.gcd(heads, 4)
    groups = heads // group_size
    received = {}
    for reach in (2, 1):
        received[reach] = shifted((byte_keys, byte_values), BYTE_AXES, reach)
    keys_all = jnp.concatenate([received[2][0][0], received[1][0][0], byte_keys[0]], axis=0)
    values_all = jnp.concatenate([received[2][1][0], received[1][1][0], byte_values[0]], axis=0)
    query_groups = byte_queries[0].reshape(rows, groups, group_size, HEAD_L).transpose(1, 0, 2, 3)
    key_groups = keys_all.reshape(3 * rows, groups, group_size, HEAD_L).transpose(1, 0, 2, 3)
    value_group_list = values_all.reshape(3 * rows, groups, group_size, HEAD_L).transpose(
        1, 0, 2, 3
    )
    qpos = jnp.arange(rows, dtype=jnp.int32)[:, None] + 2 * rows
    kpos = jnp.arange(3 * rows, dtype=jnp.int32)[None, :]
    position = lax.axis_index(BYTE_AXES)
    reachable = (kpos >= 2 * rows) | (kpos >= rows) & (position >= 1) | (position >= 2)
    allowed = (kpos <= qpos) & (kpos > qpos - 2 * rows) & reachable

    def attend(items):
        query, keys, values = items
        scores = jnp.einsum(
            "ihd,jhd->hij", query, keys, preferred_element_type=jnp.float32
        ) * HEAD_L ** (-0.5)
        scores = jnp.where(allowed[None], scores, -1e30)
        top = jnp.max(scores, axis=-1, keepdims=True)
        expo = jnp.exp(scores - top)
        weights = (expo / jnp.sum(expo, axis=-1, keepdims=True)).astype(jnp.bfloat16)
        mixed = jnp.einsum("hij,jhd->ihd", weights, values, preferred_element_type=jnp.float32)
        return mixed.astype(jnp.bfloat16)

    encoded = lax.map(attend, (query_groups, key_groups, value_group_list))
    encoded = encoded.transpose(1, 0, 2, 3).reshape(rows, width)
    starts = patch_starts[0, 0]
    nexts = jnp.concatenate([starts[1:], jnp.full((1,), rows, jnp.int32)])
    place = jnp.arange(rows, dtype=jnp.int32)[None, :]
    member = (place >= starts[:, None]) & (place < nexts[:, None])
    length = jnp.sum(member.astype(jnp.float32), axis=-1)
    summed = jnp.dot(member.astype(jnp.bfloat16), encoded, preferred_element_type=jnp.float32)
    pooled = (summed / jnp.maximum(length, 1.0)[:, None]).astype(jnp.bfloat16)
    valid = starts < rows
    pr, bl = patch_proj.shape
    lr, lc = latent_proj.shape
    wbuf = jnp.concatenate([patch_proj.reshape(-1), latent_proj.reshape(-1)])
    wbuf = lax.all_gather(wbuf, "x", axis=0)
    wbuf = lax.all_gather(wbuf, "y", axis=0)
    ndp = wbuf.shape[0] * wbuf.shape[1]
    wbuf = wbuf.reshape(ndp, -1)
    proj_cols = wbuf[:, : pr * bl].reshape(ndp * pr, bl)
    latent_row_list = wbuf[:, pr * bl :].reshape(ndp, lr, lc).transpose(1, 0, 2).reshape(lr, ndp * lc)
    patches = lax.all_gather(pooled[None], BYTE_AXES, axis=1, tiled=True)
    hidden_in = jnp.dot(patches[0], proj_cols, preferred_element_type=jnp.float32)
    activation = jax.nn.silu(hidden_in).astype(jnp.bfloat16)
    piece = activation
    latent = lax.psum_scatter(
        jnp.dot(piece, latent_row_list, preferred_element_type=jnp.float32).astype(jnp.bfloat16),
        BYTE_AXES,
        scatter_dimension=0,
        tiled=True,
    )
    cot_all = lax.all_gather(latent_cotangent, BYTE_AXES, axis=1, tiled=True)
    back = lax.dot_general(
        cot_all[0], latent_row_list, (((1,), (1,)), ((), ())), preferred_element_type=jnp.float32
    )
    sigma = jax.nn.sigmoid(hidden_in)
    act_grad = (back * sigma * (1.0 + hidden_in * (1.0 - sigma))).astype(jnp.bfloat16)
    piece = act_grad
    grads = lax.psum_scatter(
        lax.dot_general(
            piece, proj_cols, (((1,), (1,)), ((), ())), preferred_element_type=jnp.float32
        ).astype(jnp.bfloat16),
        BYTE_AXES,
        scatter_dimension=0,
        tiled=True,
    ).astype(jnp.float32)
    grads = jnp.where(valid[:, None], grads, 0.0)
    return (latent[None], grads.astype(jnp.bfloat16)[None])


def solution(mesh):
    n_dp = mesh.shape["dp"]
    n_bytes = mesh.shape["bytes"]
    side = int(round(math.sqrt(n_dp)))
    view = Mesh(
        np.asarray(mesh.devices).reshape(n_dp // side, side, n_bytes // 2, 2),
        DP_AXES + BYTE_AXES,
    )
    act = P(DP_AXES, BYTE_AXES, None)
    return jax.shard_map(
        per_device,
        mesh=view,
        in_specs=(act, act, act, act, P(DP_AXES, BYTE_AXES), P(BYTE_AXES, DP_AXES), act),
        out_specs=(act, act),
        check_vma=False,
    )
```

```python
import math

import jax
import jax.numpy as jnp
from jax import lax
import numpy as np
from jax.sharding import Mesh
from jax.sharding import PartitionSpec as P

HEAD_L = 64
BYTE_AXES = ("z", "c")
DP_AXES = ("y", "x")


def shifted(shard, axis, by):
    devices = lax.axis_size(axis)
    pairs = [(i, i + by) for i in range(devices) if 0 <= i + by < devices]
    return lax.ppermute(shard, axis, pairs)


def per_device(
    byte_queries, byte_keys, byte_values, patch_starts, patch_proj, latent_proj, latent_cotangent
):
    rows = byte_queries.shape[1]
    width = byte_queries.shape[2]
    heads = width // HEAD_L
    group_size = math.gcd(heads, 4)
    groups = heads // group_size
    received = {}
    for reach in (2, 1):
        received[reach] = shifted((byte_keys, byte_values), BYTE_AXES, reach)
    keys_all = jnp.concatenate([received[2][0][0], received[1][0][0], byte_keys[0]], axis=0)
    values_all = jnp.concatenate([received[2][1][0], received[1][1][0], byte_values[0]], axis=0)
    query_groups = byte_queries[0].reshape(rows, groups, group_size, HEAD_L).transpose(1, 0, 2, 3)
    key_groups = keys_all.reshape(3 * rows, groups, group_size, HEAD_L).transpose(1, 0, 2, 3)
    value_group_list = values_all.reshape(3 * rows, groups, group_size, HEAD_L).transpose(
        1, 0, 2, 3
    )
    qpos = jnp.arange(rows, dtype=jnp.int32)[:, None] + 2 * rows
    kpos = jnp.arange(3 * rows, dtype=jnp.int32)[None, :]
    position = lax.axis_index(BYTE_AXES)
    reachable = (kpos >= 2 * rows) | (kpos >= rows) & (position >= 1) | (position >= 2)
    allowed = (kpos <= qpos) & (kpos > qpos - 2 * rows) & reachable

    def attend(items):
        query, keys, values = items
        scores = jnp.einsum(
            "ihd,jhd->hij", query, keys, preferred_element_type=jnp.float32
        ) * HEAD_L ** (-0.5)
        scores = jnp.where(allowed[None], scores, -1e30)
        top = jnp.max(scores, axis=-1, keepdims=True)
        expo = jnp.exp(scores - top)
        weights = (expo / jnp.sum(expo, axis=-1, keepdims=True)).astype(jnp.bfloat16)
        mixed = jnp.einsum("hij,jhd->ihd", weights, values, preferred_element_type=jnp.float32)
        return mixed.astype(jnp.bfloat16)

    encoded = lax.map(attend, (query_groups, key_groups, value_group_list))
    encoded = encoded.transpose(1, 0, 2, 3).reshape(rows, width)
    starts = patch_starts[0, 0]
    nexts = jnp.concatenate([starts[1:], jnp.full((1,), rows, jnp.int32)])
    place = jnp.arange(rows, dtype=jnp.int32)[None, :]
    member = (place >= starts[:, None]) & (place < nexts[:, None])
    length = jnp.sum(member.astype(jnp.float32), axis=-1)
    summed = jnp.dot(member.astype(jnp.bfloat16), encoded, preferred_element_type=jnp.float32)
    pooled = (summed / jnp.maximum(length, 1.0)[:, None]).astype(jnp.bfloat16)
    valid = starts < rows
    pr, bl = patch_proj.shape
    lr, lc = latent_proj.shape
    wbuf = jnp.concatenate([patch_proj.reshape(-1), latent_proj.reshape(-1)])
    wbuf = lax.all_gather(wbuf, "x", axis=0)
    cot_all = lax.all_gather(latent_cotangent, BYTE_AXES, axis=1, tiled=True)
    wbuf, cot_all = lax.optimization_barrier((wbuf, cot_all))
    wbuf = lax.all_gather(wbuf, "y", axis=0)
    ndp = wbuf.shape[0] * wbuf.shape[1]
    wbuf = wbuf.reshape(ndp, -1)
    proj_cols = wbuf[:, : pr * bl].reshape(ndp * pr, bl)
    latent_row_list = wbuf[:, pr * bl :].reshape(ndp, lr, lc).transpose(1, 0, 2).reshape(lr, ndp * lc)
    patches = lax.all_gather(pooled[None], BYTE_AXES, axis=1, tiled=True)
    hidden_in = jnp.dot(patches[0], proj_cols, preferred_element_type=jnp.float32)
    activation = jax.nn.silu(hidden_in).astype(jnp.bfloat16)
    piece = activation
    latent = lax.psum_scatter(
        jnp.dot(piece, latent_row_list, preferred_element_type=jnp.float32).astype(jnp.bfloat16),
        BYTE_AXES,
        scatter_dimension=0,
        tiled=True,
    )
    back = lax.dot_general(
        cot_all[0], latent_row_list, (((1,), (1,)), ((), ())), preferred_element_type=jnp.float32
    )
    sigma = jax.nn.sigmoid(hidden_in)
    act_grad = (back * sigma * (1.0 + hidden_in * (1.0 - sigma))).astype(jnp.bfloat16)
    piece = act_grad
    grads = lax.psum_scatter(
        lax.dot_general(
            piece, proj_cols, (((1,), (1,)), ((), ())), preferred_element_type=jnp.float32
        ).astype(jnp.bfloat16),
        BYTE_AXES,
        scatter_dimension=0,
        tiled=True,
    ).astype(jnp.float32)
    grads = jnp.where(valid[:, None], grads, 0.0)
    return (latent[None], grads.astype(jnp.bfloat16)[None])


def solution(mesh):
    n_dp = mesh.shape["dp"]
    n_bytes = mesh.shape["bytes"]
    side = int(round(math.sqrt(n_dp)))
    view = Mesh(
        np.asarray(mesh.devices).reshape(n_dp // side, side, n_bytes // 2, 2),
        DP_AXES + BYTE_AXES,
    )
    act = P(DP_AXES, BYTE_AXES, None)
    return jax.shard_map(
        per_device,
        mesh=view,
        in_specs=(act, act, act, act, P(DP_AXES, BYTE_AXES), P(BYTE_AXES, DP_AXES), act),
        out_specs=(act, act),
        check_vma=False,
    )
```

```python
import math

import jax
import jax.numpy as jnp
from jax import lax
import numpy as np
from jax.sharding import Mesh
from jax.sharding import PartitionSpec as P

HEAD_L = 64
BYTE_AXES = ("z", "c")
DP_AXES = ("y", "x")


def shifted(shard, axis, by):
    devices = lax.axis_size(axis)
    pairs = [(i, i + by) for i in range(devices) if 0 <= i + by < devices]
    return lax.ppermute(shard, axis, pairs)


def per_device(
    byte_queries, byte_keys, byte_values, patch_starts, patch_proj, latent_proj, latent_cotangent
):
    rows = byte_queries.shape[1]
    width = byte_queries.shape[2]
    heads = width // HEAD_L
    group_size = math.gcd(heads, 4)
    groups = heads // group_size
    received = {}
    for reach in (2, 1):
        received[reach] = shifted((byte_keys, byte_values), BYTE_AXES, reach)
    keys_all = jnp.concatenate([received[2][0][0], received[1][0][0], byte_keys[0]], axis=0)
    values_all = jnp.concatenate([received[2][1][0], received[1][1][0], byte_values[0]], axis=0)
    query_groups = byte_queries[0].reshape(rows, groups, group_size, HEAD_L).transpose(1, 0, 2, 3)
    key_groups = keys_all.reshape(3 * rows, groups, group_size, HEAD_L).transpose(1, 0, 2, 3)
    value_group_list = values_all.reshape(3 * rows, groups, group_size, HEAD_L).transpose(
        1, 0, 2, 3
    )
    qpos = jnp.arange(rows, dtype=jnp.int32)[:, None] + 2 * rows
    kpos = jnp.arange(3 * rows, dtype=jnp.int32)[None, :]
    position = lax.axis_index(BYTE_AXES)
    reachable = (kpos >= 2 * rows) | (kpos >= rows) & (position >= 1) | (position >= 2)
    allowed = (kpos <= qpos) & (kpos > qpos - 2 * rows) & reachable

    def attend(items):
        query, keys, values = items
        scores = jnp.einsum(
            "ihd,jhd->hij", query, keys, preferred_element_type=jnp.float32
        ) * HEAD_L ** (-0.5)
        scores = jnp.where(allowed[None], scores, -1e30)
        top = jnp.max(scores, axis=-1, keepdims=True)
        expo = jnp.exp(scores - top)
        weights = (expo / jnp.sum(expo, axis=-1, keepdims=True)).astype(jnp.bfloat16)
        mixed = jnp.einsum("hij,jhd->ihd", weights, values, preferred_element_type=jnp.float32)
        return mixed.astype(jnp.bfloat16)

    encoded = lax.map(attend, (query_groups, key_groups, value_group_list))
    encoded = encoded.transpose(1, 0, 2, 3).reshape(rows, width)
    starts = patch_starts[0, 0]
    nexts = jnp.concatenate([starts[1:], jnp.full((1,), rows, jnp.int32)])
    place = jnp.arange(rows, dtype=jnp.int32)[None, :]
    member = (place >= starts[:, None]) & (place < nexts[:, None])
    length = jnp.sum(member.astype(jnp.float32), axis=-1)
    summed = jnp.dot(member.astype(jnp.bfloat16), encoded, preferred_element_type=jnp.float32)
    pooled = (summed / jnp.maximum(length, 1.0)[:, None]).astype(jnp.bfloat16)
    valid = starts < rows
    pr, bl = patch_proj.shape
    lr, lc = latent_proj.shape
    wbuf = jnp.concatenate([patch_proj.reshape(-1), latent_proj.reshape(-1)])
    wbuf = lax.all_gather(wbuf, "x", axis=0)
    cot_all = lax.all_gather(latent_cotangent, BYTE_AXES, axis=1, tiled=True)
    wbuf, cot_all = lax.optimization_barrier((wbuf, cot_all))
    wbuf = lax.all_gather(wbuf, "y", axis=0)
    ndp = wbuf.shape[0] * wbuf.shape[1]
    wbuf = wbuf.reshape(ndp, -1)
    proj_cols = wbuf[:, : pr * bl].reshape(ndp * pr, bl)
    latent_row_list = wbuf[:, pr * bl :].reshape(ndp, lr, lc).transpose(1, 0, 2).reshape(lr, ndp * lc)
    patches = lax.all_gather(pooled[None], BYTE_AXES, axis=1, tiled=True)
    hidden_in = jnp.dot(patches[0], proj_cols, preferred_element_type=jnp.float32)
    activation = jax.nn.silu(hidden_in).astype(jnp.bfloat16)
    shards = patches.shape[1] // pooled.shape[0]
    rows_of = pooled.shape[0]
    rows_pad = -(-rows_of // 8) * 8

    def padded(block_product):
        split = block_product.reshape(shards, rows_of, -1)
        split = jnp.pad(split, ((0, 0), (0, rows_pad - rows_of), (0, 0)))
        return split.reshape(shards * rows_pad, -1)

    piece = activation
    latent = lax.psum_scatter(
        padded(jnp.dot(piece, latent_row_list, preferred_element_type=jnp.float32).astype(jnp.bfloat16)),
        BYTE_AXES,
        scatter_dimension=0,
        tiled=True,
    )[:rows_of]
    back = lax.dot_general(
        cot_all[0], latent_row_list, (((1,), (1,)), ((), ())), preferred_element_type=jnp.float32
    )
    sigma = jax.nn.sigmoid(hidden_in)
    act_grad = (back * sigma * (1.0 + hidden_in * (1.0 - sigma))).astype(jnp.bfloat16)
    piece = act_grad
    grads = lax.psum_scatter(
        padded(lax.dot_general(
            piece, proj_cols, (((1,), (1,)), ((), ())), preferred_element_type=jnp.float32
        ).astype(jnp.bfloat16)),
        BYTE_AXES,
        scatter_dimension=0,
        tiled=True,
    )[:rows_of].astype(jnp.float32)
    grads = jnp.where(valid[:, None], grads, 0.0)
    return (latent[None], grads.astype(jnp.bfloat16)[None])


def solution(mesh):
    n_dp = mesh.shape["dp"]
    n_bytes = mesh.shape["bytes"]
    side = int(round(math.sqrt(n_dp)))
    view = Mesh(
        np.asarray(mesh.devices).reshape(n_dp // side, side, n_bytes // 2, 2),
        DP_AXES + BYTE_AXES,
    )
    act = P(DP_AXES, BYTE_AXES, None)
    return jax.shard_map(
        per_device,
        mesh=view,
        in_specs=(act, act, act, act, P(DP_AXES, BYTE_AXES), P(BYTE_AXES, DP_AXES), act),
        out_specs=(act, act),
        check_vma=False,
    )
```
